256 devices in a mesh: dom: 32 (over y_hi, z, core), tp: 8 (over x, y_lo).
Axes of the slice: x: 4, y: 4 (y_hi: 2, y_lo: 2; y = y_hi * 2 + y_lo), z: 8, core: 2. Of those that a mesh axis runs over, the one named last changes fastest.
Arguments:
- hidden_in: bfloat16 [448, 64, 4096], P('dom', None, 'tp'), may hold values from -6 to 6
- query_weight: bfloat16 [4096, 4096], P('dom', 'tp'), may hold values from -0.09375 to 0.09375
- segment_keys: bfloat16 [448, 64, 1024], P('dom', None, 'tp'), may hold values from -6 to 6
- segment_values: bfloat16 [448, 64, 1024], P('dom', None, 'tp'), may hold values from -6 to 6
- prefix_keys: bfloat16 [32, 256, 1024], P('dom', None, 'tp'), may hold values from -80 to 80
- prefix_values: bfloat16 [32, 256, 1024], P('dom', None, 'tp'), may hold values from -6 to 6
- ancestors: int32 [448], P('dom'), may hold values from 0 to 31, as said below
- twist_weights: float32 [448], P('dom'), may hold values from 0.25 to 4
- out_grad: bfloat16 [448, 64, 4096], P('dom', None, 'tp'), may hold values from -24 to 24
Outputs:
- grad_query_weight: bfloat16 [4096, 4096], P('dom', 'tp')
- grad_segment_keys: bfloat16 [448, 64, 1024], P('dom', None, 'tp')
- grad_segment_values: bfloat16 [448, 64, 1024], P('dom', None, 'tp')
- grad_prefix_keys: float32 [32, 256, 1024], P('dom', None, 'tp')
- grad_prefix_values: float32 [32, 256, 1024], P('dom', None, 'tp')
The draws below stay inside these ranges and needn't reach their ends.
Inputs may be any that keep to these rules, and one draw needn't show every extreme that they name: `ancestors`: among the 14 consecutive particles of one device, no ancestor is named more than 2 times, and one ancestor, the same for all devices, is named exactly 2 times on every device.
All inputs are finite; a program needn't handle non-finite values.
Results may differ from the reference program's by a relative error of at most 0.02.
The reference program's roundings to bfloat16 on the way count: a program that leaves them out, or rounds other values in their place, can miss the bound.
Values may be sent and summed in bfloat16 or wider, within the bound.
No kernel may reach another device: no remote copies, remote signals or barrier semaphores. Data moves between devices by JAX's collectives and lax.ppermute only.
A program may use at most 128 MiB of HBM per device.

```python
import math
import jax
import jax.numpy as jnp
from jax import lax

D = 4096
HQ = 32
KVH = 8
HD = 128
SEG = 64
PRE = 256
PART_DEV = 14
PARTICLES = 448
PREFIXES = 32
CAP = 2
N_DOM = 32


def draw_prefix_keys(key, part):
    shape = (PREFIXES, PRE, KVH * HD)
    first = jax.random.fold_in(key, 0)
    values = jax.random.normal(first, shape, jnp.float32)
    return jnp.clip(values, -80.0, 80.0).astype(jnp.bfloat16)


def draw_ancestors(key, part):
    owners = PARTICLES // PART_DEV
    first, second = jax.random.split(key)
    popular = jax.random.randint(first, (), 0, owners, jnp.int32)

    def one_block(block_key):
        keys = jax.random.split(block_key, 3)
        others = jax.random.permutation(keys[0], owners - 1).astype(jnp.int32)
        others = others + (others >= popular).astype(jnp.int32)
        pool = jax.random.permutation(keys[1], jnp.tile(others, CAP))
        chosen = jnp.concatenate([jnp.full((CAP,), popular, jnp.int32), pool[:PART_DEV - CAP]])
        return jax.random.permutation(keys[2], chosen)
    return jax.vmap(one_block)(jax.random.split(second, owners)).reshape(PARTICLES)


def shard_levels(own_key, shape, cuts, least, high):
    def one(axis_at, shards_of):
        draws = jax.random.uniform(jax.random.fold_in(jax.random.fold_in(own_key, 6), axis_at), (shards_of,), jnp.float32, least / len(cuts), high / len(cuts))
        return jnp.repeat(jnp.exp(draws), shape[axis_at] // shards_of).reshape((-1,) + (1,) * (len(shape) - axis_at - 1))

    loudness = one(*cuts[0])
    for cut in cuts[1:]:
        loudness = loudness * one(*cut)
    return loudness


def centred(own_key, extent, deviation, most, pieces=(), held_as=jnp.bfloat16):
    drawn = jax.random.normal(own_key, extent, jnp.float32) * deviation
    if len(pieces) > 0:
        drawn = shard_levels(own_key, extent, pieces, -0.22, 0.18) * drawn
    return jnp.clip(drawn, min=-most, max=most).astype(held_as)


def setup_inputs(seed: int = 0) -> dict:
    splits = jax.random.split(jax.random.key(seed), 10)
    hidden_in = centred(splits[0], (PARTICLES, SEG, D), 1.0, 6.0, ((0, 32), (2, 8)))
    query_weight = centred(splits[1], (D, HQ * HD), D ** -0.5, 0.09375, ((0, 32), (1, 8)))
    segment_keys = centred(splits[2], (PARTICLES, SEG, KVH * HD), 1.0, 6.0, ((0, 32), (2, 8)))
    segment_values = centred(splits[3], (PARTICLES, SEG, KVH * HD), 1.0, 6.0, ((0, 32), (2, 8)))
    prefix_keys = draw_prefix_keys(jax.random.fold_in(splits[9], 71), 0)
    prefix_values = centred(splits[5], (PREFIXES, PRE, KVH * HD), 1.0, 6.0, ((0, 32), (2, 8)))
    ancestors = draw_ancestors(jax.random.fold_in(splits[9], 71), 0)
    twist_weights = jnp.clip(jnp.exp(math.log(4.0) - 2.7725887 * jax.random.uniform(splits[7], (PARTICLES,), jnp.float32) ** shard_levels(splits[7], (PARTICLES,), ((0, 32),), -0.2, 0.2)), 0.25, 4.0)
    out_grad = centred(splits[8], (PARTICLES, SEG, HQ * HD), 4.0, 24.0, ((0, 32), (2, 8)))
    return dict(hidden_in=hidden_in, query_weight=query_weight, segment_keys=segment_keys, segment_values=segment_values, prefix_keys=prefix_keys, prefix_values=prefix_values, ancestors=ancestors, twist_weights=twist_weights, out_grad=out_grad)


def attend(queries, scaled, seg_keys, seg_values, pre_keys, pre_values):
    factor = 1.0 / math.sqrt(queries.shape[-1])
    qf = queries.astype(jnp.float32)
    sf = scaled.astype(jnp.float32)
    score_pre = jnp.einsum('bikgd,bjkd->bkgij', qf, pre_keys.astype(jnp.float32)) * factor
    score_seg = jnp.einsum('bikgd,bjkd->bkgij', qf, seg_keys.astype(jnp.float32)) * factor
    length = queries.shape[1]
    causal = lax.broadcasted_iota(jnp.int32, (length, length), 0) >= lax.broadcasted_iota(jnp.int32, (length, length), 1)
    score_seg = jnp.where(causal, score_seg, -jnp.inf)
    row_max = jnp.maximum(lax.optimization_barrier(jnp.max(score_pre, -1)), lax.optimization_barrier(jnp.max(score_seg, -1)))[..., None]
    exp_pre = jnp.exp(score_pre - row_max)
    exp_seg = jnp.exp(score_seg - row_max)
    denominator = (lax.optimization_barrier(jnp.sum(exp_pre, -1)) + lax.optimization_barrier(jnp.sum(exp_seg, -1)))[..., None]
    prob_pre = exp_pre / denominator
    prob_seg = exp_seg / denominator
    dprob_pre = jnp.einsum('bikgd,bjkd->bkgij', sf, pre_values.astype(jnp.float32))
    dprob_seg = jnp.einsum('bikgd,bjkd->bkgij', sf, seg_values.astype(jnp.float32))
    row_delta = (lax.optimization_barrier(jnp.sum(prob_pre * dprob_pre, -1)) + lax.optimization_barrier(jnp.sum(prob_seg * dprob_seg, -1)))[..., None]
    dscore_pre = (prob_pre * (dprob_pre - row_delta)).astype(jnp.bfloat16).astype(jnp.float32)
    dscore_seg = (prob_seg * (dprob_seg - row_delta)).astype(jnp.bfloat16).astype(jnp.float32)
    low_pre = prob_pre.astype(jnp.bfloat16).astype(jnp.float32)
    low_seg = prob_seg.astype(jnp.bfloat16).astype(jnp.float32)
    grad_q = (jnp.einsum('bkgij,bjkd->bikgd', dscore_pre, pre_keys.astype(jnp.float32)) + jnp.einsum('bkgij,bjkd->bikgd', dscore_seg, seg_keys.astype(jnp.float32))) * factor
    grad_pk = jnp.einsum('bkgij,bikgd->bjkd', dscore_pre, qf) * factor
    grad_pv = jnp.einsum('bkgij,bikgd->bjkd', low_pre, sf)
    grad_sk = jnp.einsum('bkgij,bikgd->bjkd', dscore_seg, qf) * factor
    grad_sv = jnp.einsum('bkgij,bikgd->bjkd', low_seg, sf)
    return (grad_q.astype(jnp.bfloat16), grad_sk.astype(jnp.bfloat16), grad_sv.astype(jnp.bfloat16), grad_pk, grad_pv)

def reference(hidden_in, query_weight, segment_keys, segment_values, prefix_keys, prefix_values, ancestors, twist_weights, out_grad):
    group_size = HQ // KVH
    width_kv = KVH * HD
    stacked = (hidden_in.reshape(N_DOM, PART_DEV, SEG, D), segment_keys.reshape(N_DOM, PART_DEV, SEG, width_kv), segment_values.reshape(N_DOM, PART_DEV, SEG, width_kv), ancestors.reshape(N_DOM, PART_DEV), twist_weights.reshape(N_DOM, PART_DEV), out_grad.reshape(N_DOM, PART_DEV, SEG, HQ * HD))
    owner_ids = jnp.arange(N_DOM, dtype=jnp.int32)

    def handle(carried, entry):
        weight_sum, key_sum, value_sum = carried
        block_in, block_keys, block_values, block_anc, block_twist, block_grad = entry
        token_rows = block_in.reshape(PART_DEV * SEG, D)
        queries = jnp.dot(token_rows, query_weight, preferred_element_type=jnp.float32).astype(jnp.bfloat16)
        scaled = (block_grad.astype(jnp.float32) * block_twist[:, None, None]).astype(jnp.bfloat16)
        pre_keys = jnp.take(prefix_keys, block_anc, axis=0).reshape(PART_DEV, PRE, KVH, HD)
        pre_values = jnp.take(prefix_values, block_anc, axis=0).reshape(PART_DEV, PRE, KVH, HD)
        grad_q, grad_sk, grad_sv, grad_pk, grad_pv = attend(queries.reshape(PART_DEV, SEG, KVH, group_size, HD), scaled.reshape(PART_DEV, SEG, KVH, group_size, HD), block_keys.reshape(PART_DEV, SEG, KVH, HD), block_values.reshape(PART_DEV, SEG, KVH, HD), pre_keys, pre_values)
        grad_rows = grad_q.reshape(PART_DEV * SEG, HQ * HD)
        partial_low = jnp.dot(token_rows.T, grad_rows, preferred_element_type=jnp.float32).astype(jnp.bfloat16)
        partial_low = lax.optimization_barrier(partial_low)
        onehot = (owner_ids[:, None] == block_anc[None, :]).astype(jnp.float32)
        key_sum = key_sum + jnp.einsum('ap,pjc->ajc', onehot, grad_pk.reshape(PART_DEV, PRE, width_kv), precision=lax.Precision.HIGHEST)
        value_sum = value_sum + jnp.einsum('ap,pjc->ajc', onehot, grad_pv.reshape(PART_DEV, PRE, width_kv), precision=lax.Precision.HIGHEST)
        return ((weight_sum + partial_low.astype(jnp.float32), key_sum, value_sum), (grad_sk, grad_sv))
    start = (jnp.zeros((D, HQ * HD), jnp.float32), jnp.zeros((N_DOM, PRE, width_kv), jnp.float32), jnp.zeros((N_DOM, PRE, width_kv), jnp.float32))
    (weight_sum, key_sum, value_sum), (all_sk, all_sv) = lax.scan(handle, start, stacked)
    return (weight_sum.astype(jnp.bfloat16), all_sk.reshape(PARTICLES, SEG, width_kv), all_sv.reshape(PARTICLES, SEG, width_kv), key_sum, value_sum)
```

```python
import math

import jax
import jax.numpy as jnp
from jax import lax
from jax.sharding import PartitionSpec as P

HD = 128


def attend(queries, scaled, seg_keys, seg_values, pre_keys, pre_values):
    factor = 1.0 / math.sqrt(queries.shape[-1])
    score_pre = (
        jnp.einsum("bikgd,bjkd->bkgij", queries, pre_keys, preferred_element_type=jnp.float32)
        * factor
    )
    score_seg = (
        jnp.einsum("bikgd,bjkd->bkgij", queries, seg_keys, preferred_element_type=jnp.float32)
        * factor
    )
    length = queries.shape[1]
    causal = lax.broadcasted_iota(jnp.int32, (length, length), 0) >= lax.broadcasted_iota(
        jnp.int32, (length, length), 1
    )
    score_seg = jnp.where(causal, score_seg, -jnp.inf)
    row_max = jnp.maximum(jnp.max(score_pre, -1), jnp.max(score_seg, -1))[..., None]
    exp_pre = jnp.exp(score_pre - row_max)
    exp_seg = jnp.exp(score_seg - row_max)
    denominator = (jnp.sum(exp_pre, -1) + jnp.sum(exp_seg, -1))[..., None]
    prob_pre = exp_pre / denominator
    prob_seg = exp_seg / denominator
    dprob_pre = jnp.einsum(
        "bikgd,bjkd->bkgij", scaled, pre_values, preferred_element_type=jnp.float32
    )
    dprob_seg = jnp.einsum(
        "bikgd,bjkd->bkgij", scaled, seg_values, preferred_element_type=jnp.float32
    )
    row_delta = (jnp.sum(prob_pre * dprob_pre, -1) + jnp.sum(prob_seg * dprob_seg, -1))[..., None]
    dscore_pre = (prob_pre * (dprob_pre - row_delta)).astype(jnp.bfloat16)
    dscore_seg = (prob_seg * (dprob_seg - row_delta)).astype(jnp.bfloat16)
    grad_q = (
        jnp.einsum("bkgij,bjkd->bikgd", dscore_pre, pre_keys, preferred_element_type=jnp.float32)
        + jnp.einsum("bkgij,bjkd->bikgd", dscore_seg, seg_keys, preferred_element_type=jnp.float32)
    ) * factor
    grad_pk = (
        jnp.einsum("bkgij,bikgd->bjkd", dscore_pre, queries, preferred_element_type=jnp.float32)
        * factor
    )
    grad_pv = jnp.einsum(
        "bkgij,bikgd->bjkd",
        prob_pre.astype(jnp.bfloat16),
        scaled,
        preferred_element_type=jnp.float32,
    )
    grad_sk = (
        jnp.einsum("bkgij,bikgd->bjkd", dscore_seg, queries, preferred_element_type=jnp.float32)
        * factor
    )
    grad_sv = jnp.einsum(
        "bkgij,bikgd->bjkd",
        prob_seg.astype(jnp.bfloat16),
        scaled,
        preferred_element_type=jnp.float32,
    )
    return (
        grad_q.astype(jnp.bfloat16),
        grad_sk.astype(jnp.bfloat16),
        grad_sv.astype(jnp.bfloat16),
        grad_pk,
        grad_pv,
    )


def local(
    hidden_in,
    query_weight,
    segment_keys,
    segment_values,
    prefix_keys,
    prefix_values,
    ancestors,
    twist_weights,
    out_grad,
):
    particles_here = hidden_in.shape[0]
    length = hidden_in.shape[1]
    owners = lax.axis_size("dom")
    features = lax.all_gather(hidden_in, "tp", axis=2, tiled=True)
    token_rows = features.reshape(particles_here * length, features.shape[2])
    width_q = query_weight.shape[1]
    width_kv = segment_keys.shape[2]
    kv_heads = width_kv // HD
    group_size = width_q // width_kv
    prefix = prefix_keys.shape[1]
    queries = jnp.dot(
        token_rows,
        lax.all_gather(query_weight, "dom", axis=0, tiled=True),
        preferred_element_type=jnp.float32,
    ).astype(jnp.bfloat16)
    queries = queries.reshape(particles_here, length, width_q)
    scaled = (out_grad.astype(jnp.float32) * twist_weights[:, None, None]).astype(jnp.bfloat16)

    own_kv = jnp.concatenate([prefix_keys, prefix_values], axis=2)
    every_kv = lax.all_to_all(
        jnp.broadcast_to(own_kv, (owners,) + own_kv.shape[1:]),
        "dom",
        split_axis=0,
        concat_axis=0,
        tiled=True,
    )
    picked = jnp.take(every_kv, ancestors, axis=0)
    pre_keys = picked[:, :, :width_kv]
    pre_values = picked[:, :, width_kv:]

    grad_q, grad_sk, grad_sv, grad_pk, grad_pv = attend(
        queries.reshape(particles_here, length, kv_heads, group_size, HD),
        scaled.reshape(particles_here, length, kv_heads, group_size, HD),
        segment_keys.reshape(particles_here, length, kv_heads, HD),
        segment_values.reshape(particles_here, length, kv_heads, HD),
        pre_keys.reshape(particles_here, prefix, kv_heads, HD),
        pre_values.reshape(particles_here, prefix, kv_heads, HD),
    )
    grad_pkv = jnp.concatenate(
        [
            grad_pk.reshape(particles_here, prefix, width_kv),
            grad_pv.reshape(particles_here, prefix, width_kv),
        ],
        axis=2,
    )
    owner_ids = jnp.arange(owners, dtype=jnp.int32)
    onehot = (owner_ids[:, None] == ancestors[None, :]).astype(jnp.float32)
    outgoing = jnp.einsum(
        "ap,pjc->ajc", onehot, grad_pkv, precision=lax.Precision.HIGHEST
    )
    incoming = lax.all_to_all(outgoing, "dom", split_axis=0, concat_axis=0, tiled=True)
    summed = jnp.sum(incoming, axis=0)
    grad_pre_keys = summed[None, :, :width_kv]
    grad_pre_values = summed[None, :, width_kv:]

    grad_seg_keys = grad_sk.reshape(particles_here, length, width_kv)
    grad_seg_values = grad_sv.reshape(particles_here, length, width_kv)
    grad_rows = grad_q.reshape(particles_here * length, width_q)
    grad_weight = lax.psum_scatter(
        jnp.einsum("tc,tq->cq", token_rows, grad_rows, preferred_element_type=jnp.float32).astype(
            jnp.bfloat16
        ),
        "dom",
        scatter_dimension=0,
        tiled=True,
    )
    return (grad_weight, grad_seg_keys, grad_seg_values, grad_pre_keys, grad_pre_values)


def solution(mesh):
    return jax.shard_map(
        local,
        mesh=mesh,
        in_specs=(
            P("dom", None, "tp"),
            P("dom", "tp"),
            P("dom", None, "tp"),
            P("dom", None, "tp"),
            P("dom", None, "tp"),
            P("dom", None, "tp"),
            P("dom"),
            P("dom"),
            P("dom", None, "tp"),
        ),
        out_specs=(
            P("dom", "tp"),
            P("dom", None, "tp"),
            P("dom", None, "tp"),
            P("dom", None, "tp"),
            P("dom", None, "tp"),
        ),
        check_vma=False,
    )
```

```python
import math

import jax
import jax.numpy as jnp
from jax import lax
from jax.sharding import PartitionSpec as P

HD = 128


def attend(queries, scaled, seg_keys, seg_values, pre_keys, pre_values):
    factor = 1.0 / math.sqrt(queries.shape[-1])
    score_pre = (
        jnp.einsum("bikgd,bjkd->bkgij", queries, pre_keys, preferred_element_type=jnp.float32)
        * factor
    )
    score_seg = (
        jnp.einsum("bikgd,bjkd->bkgij", queries, seg_keys, preferred_element_type=jnp.float32)
        * factor
    )
    length = queries.shape[1]
    causal = lax.broadcasted_iota(jnp.int32, (length, length), 0) >= lax.broadcasted_iota(
        jnp.int32, (length, length), 1
    )
    score_seg = jnp.where(causal, score_seg, -jnp.inf)
    row_max = jnp.maximum(jnp.max(score_pre, -1), jnp.max(score_seg, -1))[..., None]
    exp_pre = jnp.exp(score_pre - row_max)
    exp_seg = jnp.exp(score_seg - row_max)
    denominator = (jnp.sum(exp_pre, -1) + jnp.sum(exp_seg, -1))[..., None]
    prob_pre = exp_pre / denominator
    prob_seg = exp_seg / denominator
    dprob_pre = jnp.einsum(
        "bikgd,bjkd->bkgij", scaled, pre_values, preferred_element_type=jnp.float32
    )
    dprob_seg = jnp.einsum(
        "bikgd,bjkd->bkgij", scaled, seg_values, preferred_element_type=jnp.float32
    )
    row_delta = (jnp.sum(prob_pre * dprob_pre, -1) + jnp.sum(prob_seg * dprob_seg, -1))[..., None]
    dscore_pre = (prob_pre * (dprob_pre - row_delta)).astype(jnp.bfloat16)
    dscore_seg = (prob_seg * (dprob_seg - row_delta)).astype(jnp.bfloat16)
    grad_q = (
        jnp.einsum("bkgij,bjkd->bikgd", dscore_pre, pre_keys, preferred_element_type=jnp.float32)
        + jnp.einsum("bkgij,bjkd->bikgd", dscore_seg, seg_keys, preferred_element_type=jnp.float32)
    ) * factor
    grad_pk = (
        jnp.einsum("bkgij,bikgd->bjkd", dscore_pre, queries, preferred_element_type=jnp.float32)
        * factor
    )
    grad_pv = jnp.einsum(
        "bkgij,bikgd->bjkd",
        prob_pre.astype(jnp.bfloat16),
        scaled,
        preferred_element_type=jnp.float32,
    )
    grad_sk = (
        jnp.einsum("bkgij,bikgd->bjkd", dscore_seg, queries, preferred_element_type=jnp.float32)
        * factor
    )
    grad_sv = jnp.einsum(
        "bkgij,bikgd->bjkd",
        prob_seg.astype(jnp.bfloat16),
        scaled,
        preferred_element_type=jnp.float32,
    )
    return (
        grad_q.astype(jnp.bfloat16),
        grad_sk.astype(jnp.bfloat16),
        grad_sv.astype(jnp.bfloat16),
        grad_pk,
        grad_pv,
    )


def local(
    hidden_in,
    query_weight,
    segment_keys,
    segment_values,
    prefix_keys,
    prefix_values,
    ancestors,
    twist_weights,
    out_grad,
):
    particles_here = hidden_in.shape[0]
    length = hidden_in.shape[1]
    owners = lax.axis_size("dom")
    features = lax.all_gather(hidden_in, "tp", axis=2, tiled=True)
    token_rows = features.reshape(particles_here * length, features.shape[2])
    width_q = query_weight.shape[1]
    width_kv = segment_keys.shape[2]
    kv_heads = width_kv // HD
    group_size = width_q // width_kv
    prefix = prefix_keys.shape[1]
    every_weight = lax.all_to_all(
        jnp.broadcast_to(query_weight[None], (owners,) + query_weight.shape),
        "dom",
        split_axis=0,
        concat_axis=0,
        tiled=True,
    ).reshape(owners * query_weight.shape[0], width_q)
    queries = jnp.dot(
        token_rows,
        every_weight,
        preferred_element_type=jnp.float32,
    ).astype(jnp.bfloat16)
    queries = queries.reshape(particles_here, length, width_q)
    scaled = (out_grad.astype(jnp.float32) * twist_weights[:, None, None]).astype(jnp.bfloat16)

    own_kv = jnp.concatenate([prefix_keys, prefix_values], axis=2)
    every_kv = lax.all_to_all(
        jnp.broadcast_to(own_kv, (owners,) + own_kv.shape[1:]),
        "dom",
        split_axis=0,
        concat_axis=0,
        tiled=True,
    )
    picked = jnp.take(every_kv, ancestors, axis=0)
    pre_keys = picked[:, :, :width_kv]
    pre_values = picked[:, :, width_kv:]

    grad_q, grad_sk, grad_sv, grad_pk, grad_pv = attend(
        queries.reshape(particles_here, length, kv_heads, group_size, HD),
        scaled.reshape(particles_here, length, kv_heads, group_size, HD),
        segment_keys.reshape(particles_here, length, kv_heads, HD),
        segment_values.reshape(particles_here, length, kv_heads, HD),
        pre_keys.reshape(particles_here, prefix, kv_heads, HD),
        pre_values.reshape(particles_here, prefix, kv_heads, HD),
    )
    grad_pkv = jnp.concatenate(
        [
            grad_pk.reshape(particles_here, prefix, width_kv),
            grad_pv.reshape(particles_here, prefix, width_kv),
        ],
        axis=2,
    )
    owner_ids = jnp.arange(owners, dtype=jnp.int32)
    onehot = (owner_ids[:, None] == ancestors[None, :]).astype(jnp.float32)
    outgoing = jnp.einsum(
        "ap,pjc->ajc", onehot, grad_pkv, precision=lax.Precision.HIGHEST
    )
    incoming = lax.all_to_all(
        outgoing.astype(jnp.bfloat16), "dom", split_axis=0, concat_axis=0, tiled=True
    )
    summed = jnp.sum(incoming.astype(jnp.float32), axis=0)
    grad_pre_keys = summed[None, :, :width_kv]
    grad_pre_values = summed[None, :, width_kv:]

    grad_seg_keys = grad_sk.reshape(particles_here, length, width_kv)
    grad_seg_values = grad_sv.reshape(particles_here, length, width_kv)
    grad_rows = grad_q.reshape(particles_here * length, width_q)
    grad_weight = lax.psum_scatter(
        jnp.einsum("tc,tq->cq", token_rows, grad_rows, preferred_element_type=jnp.float32).astype(
            jnp.bfloat16
        ),
        "dom",
        scatter_dimension=0,
        tiled=True,
    )
    return (grad_weight, grad_seg_keys, grad_seg_values, grad_pre_keys, grad_pre_values)


def solution(mesh):
    return jax.shard_map(
        local,
        mesh=mesh,
        in_specs=(
            P("dom", None, "tp"),
            P("dom", "tp"),
            P("dom", None, "tp"),
            P("dom", None, "tp"),
            P("dom", None, "tp"),
            P("dom", None, "tp"),
            P("dom"),
            P("dom"),
            P("dom", None, "tp"),
        ),
        out_specs=(
            P("dom", "tp"),
            P("dom", None, "tp"),
            P("dom", None, "tp"),
            P("dom", None, "tp"),
            P("dom", None, "tp"),
        ),
        check_vma=False,
    )
```

```python
import math

import jax
import jax.numpy as jnp
from jax import lax
from jax.sharding import PartitionSpec as P

HD = 128


def attend(queries, scaled, seg_keys, seg_values, pre_keys, pre_values):
    factor = 1.0 / math.sqrt(queries.shape[-1])
    score_pre = (
        jnp.einsum("bikgd,bjkd->bkgij", queries, pre_keys, preferred_element_type=jnp.float32)
        * factor
    )
    score_seg = (
        jnp.einsum("bikgd,bjkd->bkgij", queries, seg_keys, preferred_element_type=jnp.float32)
        * factor
    )
    length = queries.shape[1]
    causal = lax.broadcasted_iota(jnp.int32, (length, length), 0) >= lax.broadcasted_iota(
        jnp.int32, (length, length), 1
    )
    score_seg = jnp.where(causal, score_seg, -jnp.inf)
    row_max = jnp.maximum(jnp.max(score_pre, -1), jnp.max(score_seg, -1))[..., None]
    exp_pre = jnp.exp(score_pre - row_max)
    exp_seg = jnp.exp(score_seg - row_max)
    denominator = (jnp.sum(exp_pre, -1) + jnp.sum(exp_seg, -1))[..., None]
    prob_pre = exp_pre / denominator
    prob_seg = exp_seg / denominator
    dprob_pre = jnp.einsum(
        "bikgd,bjkd->bkgij", scaled, pre_values, preferred_element_type=jnp.float32
    )
    dprob_seg = jnp.einsum(
        "bikgd,bjkd->bkgij", scaled, seg_values, preferred_element_type=jnp.float32
    )
    row_delta = (jnp.sum(prob_pre * dprob_pre, -1) + jnp.sum(prob_seg * dprob_seg, -1))[..., None]
    dscore_pre = (prob_pre * (dprob_pre - row_delta)).astype(jnp.bfloat16)
    dscore_seg = (prob_seg * (dprob_seg - row_delta)).astype(jnp.bfloat16)
    grad_q = (
        jnp.einsum("bkgij,bjkd->bikgd", dscore_pre, pre_keys, preferred_element_type=jnp.float32)
        + jnp.einsum("bkgij,bjkd->bikgd", dscore_seg, seg_keys, preferred_element_type=jnp.float32)
    ) * factor
    grad_pk = (
        jnp.einsum("bkgij,bikgd->bjkd", dscore_pre, queries, preferred_element_type=jnp.float32)
        * factor
    )
    grad_pv = jnp.einsum(
        "bkgij,bikgd->bjkd",
        prob_pre.astype(jnp.bfloat16),
        scaled,
        preferred_element_type=jnp.float32,
    )
    grad_sk = (
        jnp.einsum("bkgij,bikgd->bjkd", dscore_seg, queries, preferred_element_type=jnp.float32)
        * factor
    )
    grad_sv = jnp.einsum(
        "bkgij,bikgd->bjkd",
        prob_seg.astype(jnp.bfloat16),
        scaled,
        preferred_element_type=jnp.float32,
    )
    return (
        grad_q.astype(jnp.bfloat16),
        grad_sk.astype(jnp.bfloat16),
        grad_sv.astype(jnp.bfloat16),
        grad_pk,
        grad_pv,
    )


TP_RING = (0, 2, 4, 6, 7, 5, 3, 1)


def gather_ring(block):
    size = len(TP_RING)
    ahead = size // 2
    behind = size - 1 - ahead
    forward = [(TP_RING[i], TP_RING[(i + 1) % size]) for i in range(size)]
    backward = [(TP_RING[(i + 1) % size], TP_RING[i]) for i in range(size)]
    pieces = [block]
    moving = block
    for _ in range(ahead):
        moving = lax.ppermute(moving, "tp", forward)
        pieces.append(moving)
    moving = block
    for _ in range(behind):
        moving = lax.ppermute(moving, "tp", backward)
        pieces.append(moving)
    offsets = [0] + [-(s + 1) for s in range(ahead)] + [s + 1 for s in range(behind)]
    ring = jnp.array(TP_RING, jnp.int32)
    place = jnp.zeros((size,), jnp.int32).at[ring].set(jnp.arange(size, dtype=jnp.int32))
    here = place[lax.axis_index("tp")]
    order = ring[(here + jnp.array(offsets, jnp.int32)) % size]
    slot_of_offset = jnp.zeros((size,), jnp.int32).at[jnp.array(offsets, jnp.int32) % size].set(
        jnp.arange(size, dtype=jnp.int32)
    )
    inverse = slot_of_offset[(place - here) % size]
    return jnp.stack(pieces), order, inverse


def local(
    hidden_in,
    query_weight,
    segment_keys,
    segment_values,
    prefix_keys,
    prefix_values,
    ancestors,
    twist_weights,
    out_grad,
):
    particles_here = hidden_in.shape[0]
    length = hidden_in.shape[1]
    owners = lax.axis_size("dom")
    features, order, inverse = gather_ring(hidden_in)
    blocks = features.shape[0]
    width_in = hidden_in.shape[2]
    token_blocks = features.reshape(blocks, particles_here * length, width_in)
    width_q = query_weight.shape[1]
    width_kv = segment_keys.shape[2]
    kv_heads = width_kv // HD
    group_size = width_q // width_kv
    prefix = prefix_keys.shape[1]
    every_weight = lax.all_gather(query_weight, "dom", axis=0, tiled=True)
    weight_blocks = jnp.take(every_weight.reshape(blocks, width_in, width_q), order, axis=0)
    queries = jnp.einsum(
        "ktd,kdq->tq",
        token_blocks,
        weight_blocks,
        preferred_element_type=jnp.float32,
    ).astype(jnp.bfloat16)
    queries = queries.reshape(particles_here, length, width_q)
    scaled = (out_grad.astype(jnp.float32) * twist_weights[:, None, None]).astype(jnp.bfloat16)

    own_kv = jnp.concatenate([prefix_keys, prefix_values], axis=2)
    every_kv = lax.all_to_all(
        jnp.broadcast_to(own_kv, (owners,) + own_kv.shape[1:]),
        "dom",
        split_axis=0,
        concat_axis=0,
        tiled=True,
    )
    picked = jnp.take(every_kv, ancestors, axis=0)
    pre_keys = picked[:, :, :width_kv]
    pre_values = picked[:, :, width_kv:]

    grad_q, grad_sk, grad_sv, grad_pk, grad_pv = attend(
        queries.reshape(particles_here, length, kv_heads, group_size, HD),
        scaled.reshape(particles_here, length, kv_heads, group_size, HD),
        segment_keys.reshape(particles_here, length, kv_heads, HD),
        segment_values.reshape(particles_here, length, kv_heads, HD),
        pre_keys.reshape(particles_here, prefix, kv_heads, HD),
        pre_values.reshape(particles_here, prefix, kv_heads, HD),
    )
    grad_pkv = jnp.concatenate(
        [
            grad_pk.reshape(particles_here, prefix, width_kv),
            grad_pv.reshape(particles_here, prefix, width_kv),
        ],
        axis=2,
    )
    owner_ids = jnp.arange(owners, dtype=jnp.int32)
    onehot = (owner_ids[:, None] == ancestors[None, :]).astype(jnp.float32)
    outgoing = jnp.einsum(
        "ap,pjc->ajc", onehot, grad_pkv, precision=lax.Precision.HIGHEST
    )
    incoming = lax.all_to_all(
        outgoing.astype(jnp.bfloat16), "dom", split_axis=0, concat_axis=0, tiled=True
    )
    summed = jnp.sum(incoming.astype(jnp.float32), axis=0)
    grad_pre_keys = summed[None, :, :width_kv]
    grad_pre_values = summed[None, :, width_kv:]

    grad_seg_keys = grad_sk.reshape(particles_here, length, width_kv)
    grad_seg_values = grad_sv.reshape(particles_here, length, width_kv)
    grad_rows = grad_q.reshape(particles_here * length, width_q)
    partial = jnp.einsum(
        "ktd,tq->kdq", token_blocks, grad_rows, preferred_element_type=jnp.float32
    ).astype(jnp.bfloat16)
    partial = jnp.take(partial, inverse, axis=0).reshape(blocks * width_in, width_q)
    grad_weight = lax.psum_scatter(
        partial,
        "dom",
        scatter_dimension=0,
        tiled=True,
    )
    return (grad_weight, grad_seg_keys, grad_seg_values, grad_pre_keys, grad_pre_values)


def solution(mesh):
    return jax.shard_map(
        local,
        mesh=mesh,
        in_specs=(
            P("dom", None, "tp"),
            P("dom", "tp"),
            P("dom", None, "tp"),
            P("dom", None, "tp"),
            P("dom", None, "tp"),
            P("dom", None, "tp"),
            P("dom"),
            P("dom"),
            P("dom", None, "tp"),
        ),
        out_specs=(
            P("dom", "tp"),
            P("dom", None, "tp"),
            P("dom", None, "tp"),
            P("dom", None, "tp"),
            P("dom", None, "tp"),
        ),
        check_vma=False,
    )
```

```python
import math

import jax
import jax.numpy as jnp
from jax import lax
from jax.sharding import PartitionSpec as P


HD = 128


def attend(queries, scaled, seg_keys, seg_values, pre_keys, pre_values):
    factor = 1.0 / math.sqrt(queries.shape[-1])
    score_pre = (
        jnp.einsum("bikgd,bjkd->bkgij", queries, pre_keys, preferred_element_type=jnp.float32)
        * factor
    )
    score_seg = (
        jnp.einsum("bikgd,bjkd->bkgij", queries, seg_keys, preferred_element_type=jnp.float32)
        * factor
    )
    length = queries.shape[1]
    causal = lax.broadcasted_iota(jnp.int32, (length, length), 0) >= lax.broadcasted_iota(
        jnp.int32, (length, length), 1
    )
    score_seg = jnp.where(causal, score_seg, -jnp.inf)
    row_max = jnp.maximum(jnp.max(score_pre, -1), jnp.max(score_seg, -1))[..., None]
    exp_pre = jnp.exp(score_pre - row_max)
    exp_seg = jnp.exp(score_seg - row_max)
    denominator = (jnp.sum(exp_pre, -1) + jnp.sum(exp_seg, -1))[..., None]
    prob_pre = exp_pre / denominator
    prob_seg = exp_seg / denominator
    dprob_pre = jnp.einsum(
        "bikgd,bjkd->bkgij", scaled, pre_values, preferred_element_type=jnp.float32
    )
    dprob_seg = jnp.einsum(
        "bikgd,bjkd->bkgij", scaled, seg_values, preferred_element_type=jnp.float32
    )
    row_delta = (jnp.sum(prob_pre * dprob_pre, -1) + jnp.sum(prob_seg * dprob_seg, -1))[..., None]
    dscore_pre = (prob_pre * (dprob_pre - row_delta)).astype(jnp.bfloat16)
    dscore_seg = (prob_seg * (dprob_seg - row_delta)).astype(jnp.bfloat16)
    grad_q = (
        jnp.einsum("bkgij,bjkd->bikgd", dscore_pre, pre_keys, preferred_element_type=jnp.float32)
        + jnp.einsum("bkgij,bjkd->bikgd", dscore_seg, seg_keys, preferred_element_type=jnp.float32)
    ) * factor
    grad_pk = (
        jnp.einsum("bkgij,bikgd->bjkd", dscore_pre, queries, preferred_element_type=jnp.float32)
        * factor
    )
    grad_pv = jnp.einsum(
        "bkgij,bikgd->bjkd",
        prob_pre.astype(jnp.bfloat16),
        scaled,
        preferred_element_type=jnp.float32,
    )
    grad_sk = (
        jnp.einsum("bkgij,bikgd->bjkd", dscore_seg, queries, preferred_element_type=jnp.float32)
        * factor
    )
    grad_sv = jnp.einsum(
        "bkgij,bikgd->bjkd",
        prob_seg.astype(jnp.bfloat16),
        scaled,
        preferred_element_type=jnp.float32,
    )
    return (grad_q.astype(jnp.bfloat16), grad_sk, grad_sv, grad_pk, grad_pv)


TP_RING = (0, 2, 4, 6, 7, 5, 3, 1)


def gather_ring(block):
    size = len(TP_RING)
    ahead = size // 2
    behind = size - 1 - ahead
    forward = [(TP_RING[i], TP_RING[(i + 1) % size]) for i in range(size)]
    backward = [(TP_RING[(i + 1) % size], TP_RING[i]) for i in range(size)]
    pieces = [block]
    moving = block
    for _ in range(ahead):
        moving = lax.ppermute(moving, "tp", forward)
        pieces.append(moving)
    moving = block
    for _ in range(behind):
        moving = lax.ppermute(moving, "tp", backward)
        pieces.append(moving)
    offsets = [0] + [-(s + 1) for s in range(ahead)] + [s + 1 for s in range(behind)]
    ring = jnp.array(TP_RING, jnp.int32)
    place = jnp.zeros((size,), jnp.int32).at[ring].set(jnp.arange(size, dtype=jnp.int32))
    here = place[lax.axis_index("tp")]
    order = ring[(here + jnp.array(offsets, jnp.int32)) % size]
    stacked = jnp.zeros((size,) + block.shape, block.dtype)
    for slot, piece in enumerate(pieces):
        stacked = lax.dynamic_update_index_in_dim(stacked, piece, order[slot], 0)
    return stacked


def local(
    hidden_in,
    query_weight,
    segment_keys,
    segment_values,
    prefix_keys,
    prefix_values,
    ancestors,
    twist_weights,
    out_grad,
):
    particles_here = hidden_in.shape[0]
    length = hidden_in.shape[1]
    owners = lax.axis_size("dom")
    features = gather_ring(hidden_in)
    blocks = features.shape[0]
    width_in = hidden_in.shape[2]
    token_blocks = features.reshape(blocks, particles_here * length, width_in)
    width_q = query_weight.shape[1]
    width_kv = segment_keys.shape[2]
    kv_heads = width_kv // HD
    group_size = width_q // width_kv
    prefix = prefix_keys.shape[1]
    every_weight = lax.all_gather(query_weight, "dom", axis=0, tiled=True)
    weight_blocks = every_weight.reshape(blocks, width_in, width_q)
    queries = jnp.einsum(
        "ktd,kdq->tq",
        token_blocks,
        weight_blocks,
        preferred_element_type=jnp.float32,
    ).astype(jnp.bfloat16)
    queries = queries.reshape(particles_here, length, kv_heads, group_size, HD)
    scaled = (out_grad.astype(jnp.float32) * twist_weights[:, None, None]).astype(jnp.bfloat16)
    scaled = scaled.reshape(particles_here, length, kv_heads, group_size, HD)

    own_kv = jnp.concatenate([prefix_keys, prefix_values], axis=2)
    every_kv = lax.all_to_all(
        jnp.broadcast_to(own_kv, (owners,) + own_kv.shape[1:]),
        "dom",
        split_axis=0,
        concat_axis=0,
        tiled=True,
    )
    picked = jnp.take(every_kv, ancestors, axis=0)
    pre_keys = picked[:, :, :width_kv].reshape(particles_here, prefix, kv_heads, HD)
    pre_values = picked[:, :, width_kv:].reshape(particles_here, prefix, kv_heads, HD)
    seg_keys = segment_keys.reshape(particles_here, length, kv_heads, HD)
    seg_values = segment_values.reshape(particles_here, length, kv_heads, HD)

    halves = 2
    per_half = group_size // halves
    weight_parts = []
    sums = None
    for half in range(halves):
        heads = slice(half * per_half, (half + 1) * per_half)
        results = attend(
            queries[:, :, :, heads],
            scaled[:, :, :, heads],
            seg_keys,
            seg_values,
            pre_keys,
            pre_values,
        )
        grad_rows = results[0].reshape(particles_here * length, width_q // halves)
        partial = jnp.einsum(
            "ktd,tq->kdq", token_blocks, grad_rows, preferred_element_type=jnp.float32
        ).astype(jnp.bfloat16)
        if half + 1 < halves:
            partial, queries, scaled = lax.optimization_barrier((partial, queries, scaled))
        weight_parts.append(
            lax.psum_scatter(
                partial.reshape(blocks * width_in, width_q // halves),
                "dom",
                scatter_dimension=0,
                tiled=True,
            )
        )
        sums = results[1:] if sums is None else tuple(a + b for a, b in zip(sums, results[1:]))
    grad_sk, grad_sv, grad_pk, grad_pv = sums
    grad_weight = jnp.concatenate(weight_parts, axis=1)

    grad_pkv = jnp.concatenate(
        [
            grad_pk.reshape(particles_here, prefix, width_kv),
            grad_pv.reshape(particles_here, prefix, width_kv),
        ],
        axis=2,
    )
    owner_ids = jnp.arange(owners, dtype=jnp.int32)
    onehot = (owner_ids[:, None] == ancestors[None, :]).astype(jnp.float32)
    outgoing = jnp.einsum(
        "ap,pjc->ajc", onehot, grad_pkv, precision=lax.Precision.HIGHEST
    )
    incoming = lax.all_to_all(
        outgoing.astype(jnp.bfloat16), "dom", split_axis=0, concat_axis=0, tiled=True
    )
    summed = jnp.sum(incoming.astype(jnp.float32), axis=0)
    grad_pre_keys = summed[None, :, :width_kv]
    grad_pre_values = summed[None, :, width_kv:]

    grad_seg_keys = grad_sk.astype(jnp.bfloat16).reshape(particles_here, length, width_kv)
    grad_seg_values = grad_sv.astype(jnp.bfloat16).reshape(particles_here, length, width_kv)
    return (grad_weight, grad_seg_keys, grad_seg_values, grad_pre_keys, grad_pre_values)


def solution(mesh):
    return jax.shard_map(
        local,
        mesh=mesh,
        in_specs=(
            P("dom", None, "tp"),
            P("dom", "tp"),
            P("dom", None, "tp"),
            P("dom", None, "tp"),
            P("dom", None, "tp"),
            P("dom", None, "tp"),
            P("dom"),
            P("dom"),
            P("dom", None, "tp"),
        ),
        out_specs=(
            P("dom", "tp"),
            P("dom", None, "tp"),
            P("dom", None, "tp"),
            P("dom", None, "tp"),
            P("dom", None, "tp"),
        ),
        check_vma=False,
    )
```

```python
import math

import jax
import jax.numpy as jnp
from jax import lax
from jax.sharding import PartitionSpec as P


HD = 128


def attend(queries, scaled, seg_keys, seg_values, pre_keys, pre_values):
    factor = 1.0 / math.sqrt(queries.shape[-1])
    score_pre = (
        jnp.einsum("bikgd,bjkd->bkgij", queries, pre_keys, preferred_element_type=jnp.float32)
        * factor
    )
    score_seg = (
        jnp.einsum("bikgd,bjkd->bkgij", queries, seg_keys, preferred_element_type=jnp.float32)
        * factor
    )
    length = queries.shape[1]
    causal = lax.broadcasted_iota(jnp.int32, (length, length), 0) >= lax.broadcasted_iota(
        jnp.int32, (length, length), 1
    )
    score_seg = jnp.where(causal, score_seg, -jnp.inf)
    row_max = jnp.maximum(jnp.max(score_pre, -1), jnp.max(score_seg, -1))[..., None]
    exp_pre = jnp.exp(score_pre - row_max)
    exp_seg = jnp.exp(score_seg - row_max)
    denominator = (jnp.sum(exp_pre, -1) + jnp.sum(exp_seg, -1))[..., None]
    prob_pre = exp_pre / denominator
    prob_seg = exp_seg / denominator
    dprob_pre = jnp.einsum(
        "bikgd,bjkd->bkgij", scaled, pre_values, preferred_element_type=jnp.float32
    )
    dprob_seg = jnp.einsum(
        "bikgd,bjkd->bkgij", scaled, seg_values, preferred_element_type=jnp.float32
    )
    row_delta = (jnp.sum(prob_pre * dprob_pre, -1) + jnp.sum(prob_seg * dprob_seg, -1))[..., None]
    dscore_pre = (prob_pre * (dprob_pre - row_delta)).astype(jnp.bfloat16)
    dscore_seg = (prob_seg * (dprob_seg - row_delta)).astype(jnp.bfloat16)
    grad_q = (
        jnp.einsum("bkgij,bjkd->bikgd", dscore_pre, pre_keys, preferred_element_type=jnp.float32)
        + jnp.einsum("bkgij,bjkd->bikgd", dscore_seg, seg_keys, preferred_element_type=jnp.float32)
    ) * factor
    grad_pk = (
        jnp.einsum("bkgij,bikgd->bjkd", dscore_pre, queries, preferred_element_type=jnp.float32)
        * factor
    )
    grad_pv = jnp.einsum(
        "bkgij,bikgd->bjkd",
        prob_pre.astype(jnp.bfloat16),
        scaled,
        preferred_element_type=jnp.float32,
    )
    grad_sk = (
        jnp.einsum("bkgij,bikgd->bjkd", dscore_seg, queries, preferred_element_type=jnp.float32)
        * factor
    )
    grad_sv = jnp.einsum(
        "bkgij,bikgd->bjkd",
        prob_seg.astype(jnp.bfloat16),
        scaled,
        preferred_element_type=jnp.float32,
    )
    return (
        grad_q.astype(jnp.bfloat16),
        grad_sk.astype(jnp.bfloat16),
        grad_sv.astype(jnp.bfloat16),
        grad_pk,
        grad_pv,
    )


TP_RING = (0, 2, 4, 6, 7, 5, 3, 1)


def gather_ring(block):
    size = len(TP_RING)
    ahead = size // 2
    behind = size - 1 - ahead
    forward = [(TP_RING[i], TP_RING[(i + 1) % size]) for i in range(size)]
    backward = [(TP_RING[(i + 1) % size], TP_RING[i]) for i in range(size)]
    pieces = [block]
    moving = block
    for _ in range(ahead):
        moving = lax.ppermute(moving, "tp", forward)
        pieces.append(moving)
    moving = block
    for _ in range(behind):
        moving = lax.ppermute(moving, "tp", backward)
        pieces.append(moving)
    offsets = [0] + [-(s + 1) for s in range(ahead)] + [s + 1 for s in range(behind)]
    ring = jnp.array(TP_RING, jnp.int32)
    place = jnp.zeros((size,), jnp.int32).at[ring].set(jnp.arange(size, dtype=jnp.int32))
    here = place[lax.axis_index("tp")]
    order = ring[(here + jnp.array(offsets, jnp.int32)) % size]
    stacked = jnp.zeros((size,) + block.shape, block.dtype)
    for slot, piece in enumerate(pieces):
        stacked = lax.dynamic_update_index_in_dim(stacked, piece, order[slot], 0)
    return stacked


def local(
    hidden_in,
    query_weight,
    segment_keys,
    segment_values,
    prefix_keys,
    prefix_values,
    ancestors,
    twist_weights,
    out_grad,
):
    particles_here = hidden_in.shape[0]
    length = hidden_in.shape[1]
    owners = lax.axis_size("dom")
    features = gather_ring(hidden_in)
    blocks = features.shape[0]
    width_in = hidden_in.shape[2]
    token_blocks = features.reshape(blocks, particles_here * length, width_in)
    width_q = query_weight.shape[1]
    width_kv = segment_keys.shape[2]
    kv_heads = width_kv // HD
    group_size = width_q // width_kv
    prefix = prefix_keys.shape[1]
    every_weight = lax.all_gather(query_weight, "dom", axis=0, tiled=True)
    weight_blocks = every_weight.reshape(blocks, width_in, width_q)
    queries = jnp.einsum(
        "ktd,kdq->tq",
        token_blocks,
        weight_blocks,
        preferred_element_type=jnp.float32,
    ).astype(jnp.bfloat16)
    queries = queries.reshape(particles_here, length, width_q)
    scaled = (out_grad.astype(jnp.float32) * twist_weights[:, None, None]).astype(jnp.bfloat16)

    own_kv = jnp.concatenate([prefix_keys, prefix_values], axis=2)
    every_kv = lax.all_to_all(
        jnp.broadcast_to(own_kv, (owners,) + own_kv.shape[1:]),
        "dom",
        split_axis=0,
        concat_axis=0,
        tiled=True,
    )
    picked = jnp.take(every_kv, ancestors, axis=0)
    pre_keys = picked[:, :, :width_kv]
    pre_values = picked[:, :, width_kv:]

    grad_q, grad_sk, grad_sv, grad_pk, grad_pv = attend(
        queries.reshape(particles_here, length, kv_heads, group_size, HD),
        scaled.reshape(particles_here, length, kv_heads, group_size, HD),
        segment_keys.reshape(particles_here, length, kv_heads, HD),
        segment_values.reshape(particles_here, length, kv_heads, HD),
        pre_keys.reshape(particles_here, prefix, kv_heads, HD),
        pre_values.reshape(particles_here, prefix, kv_heads, HD),
    )
    grad_rows = grad_q.reshape(particles_here * length, width_q)
    partial = jnp.einsum(
        "ktd,tq->kdq", token_blocks, grad_rows, preferred_element_type=jnp.float32
    ).astype(jnp.bfloat16)
    grad_weight = lax.psum_scatter(
        partial.reshape(blocks * width_in, width_q),
        "dom",
        scatter_dimension=0,
        tiled=True,
    )
    grad_pkv = jnp.concatenate(
        [
            grad_pk.reshape(particles_here, prefix, width_kv),
            grad_pv.reshape(particles_here, prefix, width_kv),
        ],
        axis=2,
    )
    owner_ids = jnp.arange(owners, dtype=jnp.int32)
    onehot = (owner_ids[:, None] == ancestors[None, :]).astype(jnp.float32)
    outgoing = jnp.einsum(
        "ap,pjc->ajc", onehot, grad_pkv, precision=lax.Precision.HIGHEST
    )
    incoming = lax.all_to_all(
        outgoing.astype(jnp.bfloat16), "dom", split_axis=0, concat_axis=0, tiled=True
    )
    summed = jnp.sum(incoming.astype(jnp.float32), axis=0)
    grad_pre_keys = summed[None, :, :width_kv]
    grad_pre_values = summed[None, :, width_kv:]
    grad_seg_keys = grad_sk.reshape(particles_here, length, width_kv)
    grad_seg_values = grad_sv.reshape(particles_here, length, width_kv)
    return (grad_weight, grad_seg_keys, grad_seg_values, grad_pre_keys, grad_pre_values)


def solution(mesh):
    return jax.shard_map(
        local,
        mesh=mesh,
        in_specs=(
            P("dom", None, "tp"),
            P("dom", "tp"),
            P("dom", None, "tp"),
            P("dom", None, "tp"),
            P("dom", None, "tp"),
            P("dom", None, "tp"),
            P("dom"),
            P("dom"),
            P("dom", None, "tp"),
        ),
        out_specs=(
            P("dom", "tp"),
            P("dom", None, "tp"),
            P("dom", None, "tp"),
            P("dom", None, "tp"),
            P("dom", None, "tp"),
        ),
        check_vma=False,
    )
```

```python
import math

import jax
import jax.numpy as jnp
from jax import lax
from jax.sharding import PartitionSpec as P


HD = 128
DOM = ("dh", "dc")


def attend(queries, scaled, seg_keys, seg_values, pre_keys, pre_values):
    factor = 1.0 / math.sqrt(queries.shape[-1])
    score_pre = (
        jnp.einsum("bikgd,bjkd->bkgij", queries, pre_keys, preferred_element_type=jnp.float32)
        * factor
    )
    score_seg = (
        jnp.einsum("bikgd,bjkd->bkgij", queries, seg_keys, preferred_element_type=jnp.float32)
        * factor
    )
    length = queries.shape[1]
    causal = lax.broadcasted_iota(jnp.int32, (length, length), 0) >= lax.broadcasted_iota(
        jnp.int32, (length, length), 1
    )
    score_seg = jnp.where(causal, score_seg, -jnp.inf)
    row_max = jnp.maximum(jnp.max(score_pre, -1), jnp.max(score_seg, -1))[..., None]
    exp_pre = jnp.exp(score_pre - row_max)
    exp_seg = jnp.exp(score_seg - row_max)
    denominator = (jnp.sum(exp_pre, -1) + jnp.sum(exp_seg, -1))[..., None]
    prob_pre = exp_pre / denominator
    prob_seg = exp_seg / denominator
    dprob_pre = jnp.einsum(
        "bikgd,bjkd->bkgij", scaled, pre_values, preferred_element_type=jnp.float32
    )
    dprob_seg = jnp.einsum(
        "bikgd,bjkd->bkgij", scaled, seg_values, preferred_element_type=jnp.float32
    )
    row_delta = (jnp.sum(prob_pre * dprob_pre, -1) + jnp.sum(prob_seg * dprob_seg, -1))[..., None]
    dscore_pre = (prob_pre * (dprob_pre - row_delta)).astype(jnp.bfloat16)
    dscore_seg = (prob_seg * (dprob_seg - row_delta)).astype(jnp.bfloat16)
    grad_q = (
        jnp.einsum("bkgij,bjkd->bikgd", dscore_pre, pre_keys, preferred_element_type=jnp.float32)
        + jnp.einsum("bkgij,bjkd->bikgd", dscore_seg, seg_keys, preferred_element_type=jnp.float32)
    ) * factor
    grad_pk = (
        jnp.einsum("bkgij,bikgd->bjkd", dscore_pre, queries, preferred_element_type=jnp.float32)
        * factor
    )
    grad_pv = jnp.einsum(
        "bkgij,bikgd->bjkd",
        prob_pre.astype(jnp.bfloat16),
        scaled,
        preferred_element_type=jnp.float32,
    )
    grad_sk = (
        jnp.einsum("bkgij,bikgd->bjkd", dscore_seg, queries, preferred_element_type=jnp.float32)
        * factor
    )
    grad_sv = jnp.einsum(
        "bkgij,bikgd->bjkd",
        prob_seg.astype(jnp.bfloat16),
        scaled,
        preferred_element_type=jnp.float32,
    )
    return (
        grad_q.astype(jnp.bfloat16),
        grad_sk.astype(jnp.bfloat16),
        grad_sv.astype(jnp.bfloat16),
        grad_pk,
        grad_pv,
    )


TP_RING = (0, 2, 4, 6, 7, 5, 3, 1)


def gather_ring(block):
    size = len(TP_RING)
    ahead = size // 2
    behind = size - 1 - ahead
    forward = [(TP_RING[i], TP_RING[(i + 1) % size]) for i in range(size)]
    backward = [(TP_RING[(i + 1) % size], TP_RING[i]) for i in range(size)]
    pieces = [block]
    moving = block
    for _ in range(ahead):
        moving = lax.ppermute(moving, "tp", forward)
        pieces.append(moving)
    moving = block
    for _ in range(behind):
        moving = lax.ppermute(moving, "tp", backward)
        pieces.append(moving)
    offsets = [0] + [-(s + 1) for s in range(ahead)] + [s + 1 for s in range(behind)]
    ring = jnp.array(TP_RING, jnp.int32)
    place = jnp.zeros((size,), jnp.int32).at[ring].set(jnp.arange(size, dtype=jnp.int32))
    here = place[lax.axis_index("tp")]
    order = ring[(here + jnp.array(offsets, jnp.int32)) % size]
    stacked = jnp.zeros((size,) + block.shape, block.dtype)
    for slot, piece in enumerate(pieces):
        stacked = lax.dynamic_update_index_in_dim(stacked, piece, order[slot], 0)
    return stacked


def pair_sum(block):
    mine = lax.axis_index("dc")
    kept = lax.dynamic_index_in_dim(block, mine, axis=1, keepdims=False)
    sent = lax.dynamic_index_in_dim(block, 1 - mine, axis=1, keepdims=False)
    other = lax.ppermute(sent, "dc", [(0, 1), (1, 0)])
    return kept.astype(jnp.float32) + other.astype(jnp.float32)


def local(
    hidden_in,
    query_weight,
    segment_keys,
    segment_values,
    prefix_keys,
    prefix_values,
    ancestors,
    twist_weights,
    out_grad,
):
    particles_here = hidden_in.shape[0]
    length = hidden_in.shape[1]
    owners = lax.axis_size(DOM)
    features = gather_ring(hidden_in)
    blocks = features.shape[0]
    width_in = hidden_in.shape[2]
    token_blocks = features.reshape(blocks, particles_here * length, width_in)
    width_q = query_weight.shape[1]
    width_kv = segment_keys.shape[2]
    kv_heads = width_kv // HD
    group_size = width_q // width_kv
    prefix = prefix_keys.shape[1]
    every_weight = lax.all_gather(query_weight, DOM, axis=0, tiled=True)
    weight_blocks = every_weight.reshape(blocks, width_in, width_q)
    queries = jnp.einsum(
        "ktd,kdq->tq",
        token_blocks,
        weight_blocks,
        preferred_element_type=jnp.float32,
    ).astype(jnp.bfloat16)
    queries = queries.reshape(particles_here, length, width_q)
    scaled = (out_grad.astype(jnp.float32) * twist_weights[:, None, None]).astype(jnp.bfloat16)

    own_kv = jnp.concatenate([prefix_keys, prefix_values], axis=2)
    every_kv = lax.all_to_all(
        jnp.broadcast_to(own_kv, (owners,) + own_kv.shape[1:]),
        DOM,
        split_axis=0,
        concat_axis=0,
        tiled=True,
    )
    picked = jnp.take(every_kv, ancestors, axis=0)
    pre_keys = picked[:, :, :width_kv]
    pre_values = picked[:, :, width_kv:]

    grad_q, grad_sk, grad_sv, grad_pk, grad_pv = attend(
        queries.reshape(particles_here, length, kv_heads, group_size, HD),
        scaled.reshape(particles_here, length, kv_heads, group_size, HD),
        segment_keys.reshape(particles_here, length, kv_heads, HD),
        segment_values.reshape(particles_here, length, kv_heads, HD),
        pre_keys.reshape(particles_here, prefix, kv_heads, HD),
        pre_values.reshape(particles_here, prefix, kv_heads, HD),
    )
    grad_rows = grad_q.reshape(particles_here * length, width_q)
    partial = jnp.einsum(
        "ktd,tq->kdq", token_blocks, grad_rows, preferred_element_type=jnp.float32
    ).astype(jnp.bfloat16)
    chips = lax.axis_size("dh")
    cores = lax.axis_size("dc")
    chip_sum = pair_sum(
        partial.reshape(chips, cores, blocks * width_in // owners, width_q)
    )
    grad_weight = lax.psum_scatter(
        chip_sum.reshape(chips * blocks * width_in // owners, width_q),
        "dh",
        scatter_dimension=0,
        tiled=True,
    ).astype(jnp.bfloat16)
    grad_pkv = jnp.concatenate(
        [
            grad_pk.reshape(particles_here, prefix, width_kv),
            grad_pv.reshape(particles_here, prefix, width_kv),
        ],
        axis=2,
    )
    owner_ids = jnp.arange(owners, dtype=jnp.int32)
    onehot = (owner_ids[:, None] == ancestors[None, :]).astype(jnp.float32)
    outgoing = jnp.einsum(
        "ap,pjc->ajc", onehot, grad_pkv, precision=lax.Precision.HIGHEST
    )
    on_chip = pair_sum(outgoing.reshape((chips, cores) + outgoing.shape[1:]))
    incoming = lax.all_to_all(
        on_chip.astype(jnp.bfloat16),
        "dh",
        split_axis=0,
        concat_axis=0,
        tiled=True,
    )
    summed = jnp.sum(incoming.astype(jnp.float32), axis=0)
    grad_pre_keys = summed[None, :, :width_kv]
    grad_pre_values = summed[None, :, width_kv:]
    grad_seg_keys = grad_sk.reshape(particles_here, length, width_kv)
    grad_seg_values = grad_sv.reshape(particles_here, length, width_kv)
    return (grad_weight, grad_seg_keys, grad_seg_values, grad_pre_keys, grad_pre_values)


def solution(mesh):
    split = jax.sharding.Mesh(
        mesh.devices.reshape(mesh.shape["dom"] // 2, 2, mesh.shape["tp"]), ("dh", "dc", "tp")
    )
    return jax.shard_map(
        local,
        mesh=split,
        in_specs=(
            P(DOM, None, "tp"),
            P(DOM, "tp"),
            P(DOM, None, "tp"),
            P(DOM, None, "tp"),
            P(DOM, None, "tp"),
            P(DOM, None, "tp"),
            P(DOM),
            P(DOM),
            P(DOM, None, "tp"),
        ),
        out_specs=(
            P(DOM, "tp"),
            P(DOM, None, "tp"),
            P(DOM, None, "tp"),
            P(DOM, None, "tp"),
            P(DOM, None, "tp"),
        ),
        check_vma=False,
    )
```

```python
import math

import jax
import jax.numpy as jnp
from jax import lax
from jax.sharding import PartitionSpec as P


HD = 128
DOM = ("dh", "dc")


def attend(queries, scaled, seg_keys, seg_values, pre_keys, pre_values):
    factor = 1.0 / math.sqrt(queries.shape[-1])
    score_pre = (
        jnp.einsum("bikgd,bjkd->bkgij", queries, pre_keys, preferred_element_type=jnp.float32)
        * factor
    )
    score_seg = (
        jnp.einsum("bikgd,bjkd->bkgij", queries, seg_keys, preferred_element_type=jnp.float32)
        * factor
    )
    length = queries.shape[1]
    causal = lax.broadcasted_iota(jnp.int32, (length, length), 0) >= lax.broadcasted_iota(
        jnp.int32, (length, length), 1
    )
    score_seg = jnp.where(causal, score_seg, -jnp.inf)
    row_max = jnp.maximum(jnp.max(score_pre, -1), jnp.max(score_seg, -1))[..., None]
    exp_pre = jnp.exp(score_pre - row_max)
    exp_seg = jnp.exp(score_seg - row_max)
    denominator = (jnp.sum(exp_pre, -1) + jnp.sum(exp_seg, -1))[..., None]
    prob_pre = exp_pre / denominator
    prob_seg = exp_seg / denominator
    dprob_pre = jnp.einsum(
        "bikgd,bjkd->bkgij", scaled, pre_values, preferred_element_type=jnp.float32
    )
    dprob_seg = jnp.einsum(
        "bikgd,bjkd->bkgij", scaled, seg_values, preferred_element_type=jnp.float32
    )
    row_delta = (jnp.sum(prob_pre * dprob_pre, -1) + jnp.sum(prob_seg * dprob_seg, -1))[..., None]
    dscore_pre = (prob_pre * (dprob_pre - row_delta)).astype(jnp.bfloat16)
    dscore_seg = (prob_seg * (dprob_seg - row_delta)).astype(jnp.bfloat16)
    grad_q = (
        jnp.einsum("bkgij,bjkd->bikgd", dscore_pre, pre_keys, preferred_element_type=jnp.float32)
        + jnp.einsum("bkgij,bjkd->bikgd", dscore_seg, seg_keys, preferred_element_type=jnp.float32)
    ) * factor
    grad_pk = (
        jnp.einsum("bkgij,bikgd->bjkd", dscore_pre, queries, preferred_element_type=jnp.float32)
        * factor
    )
    grad_pv = jnp.einsum(
        "bkgij,bikgd->bjkd",
        prob_pre.astype(jnp.bfloat16),
        scaled,
        preferred_element_type=jnp.float32,
    )
    grad_sk = (
        jnp.einsum("bkgij,bikgd->bjkd", dscore_seg, queries, preferred_element_type=jnp.float32)
        * factor
    )
    grad_sv = jnp.einsum(
        "bkgij,bikgd->bjkd",
        prob_seg.astype(jnp.bfloat16),
        scaled,
        preferred_element_type=jnp.float32,
    )
    return (
        grad_q.astype(jnp.bfloat16),
        grad_sk.astype(jnp.bfloat16),
        grad_sv.astype(jnp.bfloat16),
        grad_pk,
        grad_pv,
    )


TP_RING = (0, 2, 4, 6, 7, 5, 3, 1)


def gather_ring(block):
    size = len(TP_RING)
    ahead = size // 2
    behind = size - 1 - ahead
    forward = [(TP_RING[i], TP_RING[(i + 1) % size]) for i in range(size)]
    backward = [(TP_RING[(i + 1) % size], TP_RING[i]) for i in range(size)]
    pieces = [block]
    moving = block
    for _ in range(ahead):
        moving = lax.ppermute(moving, "tp", forward)
        pieces.append(moving)
    moving = block
    for _ in range(behind):
        moving = lax.ppermute(moving, "tp", backward)
        pieces.append(moving)
    offsets = [0] + [-(s + 1) for s in range(ahead)] + [s + 1 for s in range(behind)]
    ring = jnp.array(TP_RING, jnp.int32)
    place = jnp.zeros((size,), jnp.int32).at[ring].set(jnp.arange(size, dtype=jnp.int32))
    here = place[lax.axis_index("tp")]
    order = ring[(here + jnp.array(offsets, jnp.int32)) % size]
    stacked = jnp.zeros((size,) + block.shape, block.dtype)
    for slot, piece in enumerate(pieces):
        stacked = lax.dynamic_update_index_in_dim(stacked, piece, order[slot], 0)
    return stacked


def pair_sum(block):
    mine = lax.axis_index("dc")
    kept = lax.dynamic_index_in_dim(block, mine, axis=1, keepdims=False)
    sent = lax.dynamic_index_in_dim(block, 1 - mine, axis=1, keepdims=False)
    other = lax.ppermute(sent, "dc", [(0, 1), (1, 0)])
    return kept.astype(jnp.float32) + other.astype(jnp.float32)


def local(
    hidden_in,
    query_weight,
    segment_keys,
    segment_values,
    prefix_keys,
    prefix_values,
    ancestors,
    twist_weights,
    out_grad,
):
    particles_here = hidden_in.shape[0]
    length = hidden_in.shape[1]
    owners = lax.axis_size(DOM)
    features = gather_ring(hidden_in)
    blocks = features.shape[0]
    width_in = hidden_in.shape[2]
    token_blocks = features.reshape(blocks, particles_here * length, width_in)
    width_q = query_weight.shape[1]
    width_kv = segment_keys.shape[2]
    kv_heads = width_kv // HD
    group_size = width_q // width_kv
    prefix = prefix_keys.shape[1]
    every_weight = lax.all_gather(query_weight, DOM, axis=0, tiled=True)
    weight_blocks = every_weight.reshape(blocks, width_in, width_q)
    queries = jnp.einsum(
        "ktd,kdq->tq",
        token_blocks,
        weight_blocks,
        preferred_element_type=jnp.float32,
    ).astype(jnp.bfloat16)
    queries = queries.reshape(particles_here, length, width_q)
    scaled = (out_grad.astype(jnp.float32) * twist_weights[:, None, None]).astype(jnp.bfloat16)

    chips = lax.axis_size("dh")
    cores = lax.axis_size("dc")
    own_kv = jnp.concatenate([prefix_keys, prefix_values], axis=2)
    half_kv = lax.all_to_all(
        jnp.broadcast_to(own_kv, (chips,) + own_kv.shape[1:]),
        "dh",
        split_axis=0,
        concat_axis=0,
        tiled=True,
    )
    other_kv = lax.ppermute(half_kv, "dc", [(0, 1), (1, 0)])
    on_this_core = (ancestors % cores == lax.axis_index("dc"))[:, None, None]
    picked = jnp.where(
        on_this_core,
        jnp.take(half_kv, ancestors // cores, axis=0),
        jnp.take(other_kv, ancestors // cores, axis=0),
    )
    pre_keys = picked[:, :, :width_kv]
    pre_values = picked[:, :, width_kv:]

    grad_q, grad_sk, grad_sv, grad_pk, grad_pv = attend(
        queries.reshape(particles_here, length, kv_heads, group_size, HD),
        scaled.reshape(particles_here, length, kv_heads, group_size, HD),
        segment_keys.reshape(particles_here, length, kv_heads, HD),
        segment_values.reshape(particles_here, length, kv_heads, HD),
        pre_keys.reshape(particles_here, prefix, kv_heads, HD),
        pre_values.reshape(particles_here, prefix, kv_heads, HD),
    )
    grad_rows = grad_q.reshape(particles_here * length, width_q)
    partial = jnp.einsum(
        "ktd,tq->kdq", token_blocks, grad_rows, preferred_element_type=jnp.float32
    ).astype(jnp.bfloat16)
    grad_weight = lax.psum_scatter(
        partial.reshape(blocks * width_in, width_q),
        DOM,
        scatter_dimension=0,
        tiled=True,
    )
    grad_pkv = jnp.concatenate(
        [
            grad_pk.reshape(particles_here, prefix, width_kv),
            grad_pv.reshape(particles_here, prefix, width_kv),
        ],
        axis=2,
    )
    owner_ids = jnp.arange(owners, dtype=jnp.int32)
    onehot = (owner_ids[:, None] == ancestors[None, :]).astype(jnp.float32)
    outgoing = jnp.einsum(
        "ap,pjc->ajc", onehot, grad_pkv, precision=lax.Precision.HIGHEST
    )
    on_chip = pair_sum(outgoing.reshape((chips, cores) + outgoing.shape[1:]))
    incoming = lax.all_to_all(
        on_chip.astype(jnp.bfloat16),
        "dh",
        split_axis=0,
        concat_axis=0,
        tiled=True,
    )
    summed = jnp.sum(incoming.astype(jnp.float32), axis=0)
    grad_pre_keys = summed[None, :, :width_kv]
    grad_pre_values = summed[None, :, width_kv:]
    grad_seg_keys = grad_sk.reshape(particles_here, length, width_kv)
    grad_seg_values = grad_sv.reshape(particles_here, length, width_kv)
    return (grad_weight, grad_seg_keys, grad_seg_values, grad_pre_keys, grad_pre_values)


def solution(mesh):
    split = jax.sharding.Mesh(
        mesh.devices.reshape(mesh.shape["dom"] // 2, 2, mesh.shape["tp"]), ("dh", "dc", "tp")
    )
    return jax.shard_map(
        local,
        mesh=split,
        in_specs=(
            P(DOM, None, "tp"),
            P(DOM, "tp"),
            P(DOM, None, "tp"),
            P(DOM, None, "tp"),
            P(DOM, None, "tp"),
            P(DOM, None, "tp"),
            P(DOM),
            P(DOM),
            P(DOM, None, "tp"),
        ),
        out_specs=(
            P(DOM, "tp"),
            P(DOM, None, "tp"),
            P(DOM, None, "tp"),
            P(DOM, None, "tp"),
            P(DOM, None, "tp"),
        ),
        check_vma=False,
    )
```

```python
import math

import jax
import jax.numpy as jnp
from jax import lax
from jax.sharding import PartitionSpec as P

HD = 128
DOM = ("dh", "dc")


def attend(queries, scaled, seg_keys, seg_values, pre_keys, pre_values):
    factor = 1.0 / math.sqrt(queries.shape[-1])
    score_pre = (
        jnp.einsum("bikgd,bjkd->bkgij", queries, pre_keys, preferred_element_type=jnp.float32)
        * factor
    )
    score_seg = (
        jnp.einsum("bikgd,bjkd->bkgij", queries, seg_keys, preferred_element_type=jnp.float32)
        * factor
    )
    length = queries.shape[1]
    causal = lax.broadcasted_iota(jnp.int32, (length, length), 0) >= lax.broadcasted_iota(
        jnp.int32, (length, length), 1
    )
    score_seg = jnp.where(causal, score_seg, -jnp.inf)
    row_max = jnp.maximum(jnp.max(score_pre, -1), jnp.max(score_seg, -1))[..., None]
    exp_pre = jnp.exp(score_pre - row_max)
    exp_seg = jnp.exp(score_seg - row_max)
    denominator = (jnp.sum(exp_pre, -1) + jnp.sum(exp_seg, -1))[..., None]
    prob_pre = exp_pre / denominator
    prob_seg = exp_seg / denominator
    dprob_pre = jnp.einsum(
        "bikgd,bjkd->bkgij", scaled, pre_values, preferred_element_type=jnp.float32
    )
    dprob_seg = jnp.einsum(
        "bikgd,bjkd->bkgij", scaled, seg_values, preferred_element_type=jnp.float32
    )
    row_delta = (jnp.sum(prob_pre * dprob_pre, -1) + jnp.sum(prob_seg * dprob_seg, -1))[..., None]
    dscore_pre = (prob_pre * (dprob_pre - row_delta)).astype(jnp.bfloat16)
    dscore_seg = (prob_seg * (dprob_seg - row_delta)).astype(jnp.bfloat16)
    grad_q = (
        jnp.einsum("bkgij,bjkd->bikgd", dscore_pre, pre_keys, preferred_element_type=jnp.float32)
        + jnp.einsum("bkgij,bjkd->bikgd", dscore_seg, seg_keys, preferred_element_type=jnp.float32)
    ) * factor
    grad_pk = (
        jnp.einsum("bkgij,bikgd->bjkd", dscore_pre, queries, preferred_element_type=jnp.float32)
        * factor
    )
    grad_pv = jnp.einsum(
        "bkgij,bikgd->bjkd",
        prob_pre.astype(jnp.bfloat16),
        scaled,
        preferred_element_type=jnp.float32,
    )
    grad_sk = (
        jnp.einsum("bkgij,bikgd->bjkd", dscore_seg, queries, preferred_element_type=jnp.float32)
        * factor
    )
    grad_sv = jnp.einsum(
        "bkgij,bikgd->bjkd",
        prob_seg.astype(jnp.bfloat16),
        scaled,
        preferred_element_type=jnp.float32,
    )
    return (
        grad_q.astype(jnp.bfloat16),
        grad_sk.astype(jnp.bfloat16),
        grad_sv.astype(jnp.bfloat16),
        grad_pk,
        grad_pv,
    )


TP_RING = (0, 2, 4, 6, 7, 5, 3, 1)


def gather_ring(block):
    size = len(TP_RING)
    ahead = size // 2
    behind = size - 1 - ahead
    forward = [(TP_RING[i], TP_RING[(i + 1) % size]) for i in range(size)]
    backward = [(TP_RING[(i + 1) % size], TP_RING[i]) for i in range(size)]
    pieces = [block]
    moving = block
    for _ in range(ahead):
        moving = lax.ppermute(moving, "tp", forward)
        pieces.append(moving)
    moving = block
    for _ in range(behind):
        moving = lax.ppermute(moving, "tp", backward)
        pieces.append(moving)
    offsets = [0] + [-(s + 1) for s in range(ahead)] + [s + 1 for s in range(behind)]
    ring = jnp.array(TP_RING, jnp.int32)
    place = jnp.zeros((size,), jnp.int32).at[ring].set(jnp.arange(size, dtype=jnp.int32))
    here = place[lax.axis_index("tp")]
    order = ring[(here + jnp.array(offsets, jnp.int32)) % size]
    stacked = jnp.zeros((size,) + block.shape, block.dtype)
    for slot, piece in enumerate(pieces):
        stacked = lax.dynamic_update_index_in_dim(stacked, piece, order[slot], 0)
    return stacked


def pair_sum(block, axis):
    mine = lax.axis_index("dc")
    kept = lax.dynamic_index_in_dim(block, mine, axis=axis, keepdims=False)
    sent = lax.dynamic_index_in_dim(block, 1 - mine, axis=axis, keepdims=False)
    other = lax.ppermute(sent, "dc", [(0, 1), (1, 0)])
    return kept.astype(jnp.float32) + other.astype(jnp.float32)


def local(
    hidden_in,
    query_weight,
    segment_keys,
    segment_values,
    prefix_keys,
    prefix_values,
    ancestors,
    twist_weights,
    out_grad,
):
    particles_here = hidden_in.shape[0]
    length = hidden_in.shape[1]
    owners = lax.axis_size(DOM)
    features = gather_ring(hidden_in)
    blocks = features.shape[0]
    width_in = hidden_in.shape[2]
    token_blocks = features.reshape(blocks, particles_here * length, width_in)
    width_q = query_weight.shape[1]
    width_kv = segment_keys.shape[2]
    kv_heads = width_kv // HD
    group_size = width_q // width_kv
    prefix = prefix_keys.shape[1]
    every_weight = lax.all_gather(query_weight, DOM, axis=0, tiled=True)
    weight_blocks = every_weight.reshape(blocks, width_in, width_q)
    queries = jnp.einsum(
        "ktd,kdq->tq",
        token_blocks,
        weight_blocks,
        preferred_element_type=jnp.float32,
    ).astype(jnp.bfloat16)
    queries = queries.reshape(particles_here, length, width_q)
    scaled = (out_grad.astype(jnp.float32) * twist_weights[:, None, None]).astype(jnp.bfloat16)

    chips = lax.axis_size("dh")
    cores = lax.axis_size("dc")
    own_kv = jnp.concatenate([prefix_keys, prefix_values], axis=2)
    half_kv = lax.all_to_all(
        jnp.broadcast_to(own_kv, (chips,) + own_kv.shape[1:]),
        "dh",
        split_axis=0,
        concat_axis=0,
        tiled=True,
    )
    other_kv = lax.ppermute(half_kv, "dc", [(0, 1), (1, 0)])
    on_this_core = (ancestors % cores == lax.axis_index("dc"))[:, None, None]
    picked = jnp.where(
        on_this_core,
        jnp.take(half_kv, ancestors // cores, axis=0),
        jnp.take(other_kv, ancestors // cores, axis=0),
    )
    pre_keys = picked[:, :, :width_kv]
    pre_values = picked[:, :, width_kv:]

    grad_q, grad_sk, grad_sv, grad_pk, grad_pv = attend(
        queries.reshape(particles_here, length, kv_heads, group_size, HD),
        scaled.reshape(particles_here, length, kv_heads, group_size, HD),
        segment_keys.reshape(particles_here, length, kv_heads, HD),
        segment_values.reshape(particles_here, length, kv_heads, HD),
        pre_keys.reshape(particles_here, prefix, kv_heads, HD),
        pre_values.reshape(particles_here, prefix, kv_heads, HD),
    )
    grad_rows = grad_q.reshape(particles_here * length, width_q)
    partial = jnp.einsum(
        "ktd,tq->kdq", token_blocks, grad_rows, preferred_element_type=jnp.float32
    ).astype(jnp.bfloat16)
    w_pair = pair_sum(partial.reshape(chips, cores, blocks * width_in // owners, width_q), 1)
    grad_pkv = jnp.concatenate(
        [
            grad_pk.reshape(particles_here, prefix, width_kv),
            grad_pv.reshape(particles_here, prefix, width_kv),
        ],
        axis=2,
    )
    core_major = jnp.arange(owners, dtype=jnp.int32).reshape(chips, cores).T.reshape(owners)
    onehot = (core_major[:, None] == ancestors[None, :]).astype(jnp.float32)
    outgoing = jnp.einsum(
        "ap,pjc->ajc", onehot, grad_pkv, precision=lax.Precision.HIGHEST
    )
    p_pair = pair_sum(outgoing.reshape((cores, chips) + outgoing.shape[1:]), 0)
    w_cols = w_pair.shape[1] * w_pair.shape[2]
    payload = jnp.concatenate(
        [w_pair.reshape(chips, w_cols), p_pair.reshape(chips, -1)], axis=1
    ).astype(jnp.bfloat16)
    incoming = lax.all_to_all(payload, "dh", split_axis=0, concat_axis=0, tiled=True)
    summed = jnp.sum(incoming.astype(jnp.float32), axis=0)
    grad_weight = summed[:w_cols].reshape(w_pair.shape[1:]).astype(jnp.bfloat16)
    pre_sum = summed[w_cols:].reshape(prefix, 2 * width_kv)
    grad_pre_keys = pre_sum[None, :, :width_kv]
    grad_pre_values = pre_sum[None, :, width_kv:]
    grad_seg_keys = grad_sk.reshape(particles_here, length, width_kv)
    grad_seg_values = grad_sv.reshape(particles_here, length, width_kv)
    return (grad_weight, grad_seg_keys, grad_seg_values, grad_pre_keys, grad_pre_values)


def solution(mesh):
    split = jax.sharding.Mesh(
        mesh.devices.reshape(mesh.shape["dom"] // 2, 2, mesh.shape["tp"]), ("dh", "dc", "tp")
    )
    return jax.shard_map(
        local,
        mesh=split,
        in_specs=(
            P(DOM, None, "tp"),
            P(DOM, "tp"),
            P(DOM, None, "tp"),
            P(DOM, None, "tp"),
            P(DOM, None, "tp"),
            P(DOM, None, "tp"),
            P(DOM),
            P(DOM),
            P(DOM, None, "tp"),
        ),
        out_specs=(
            P(DOM, "tp"),
            P(DOM, None, "tp"),
            P(DOM, None, "tp"),
            P(DOM, None, "tp"),
            P(DOM, None, "tp"),
        ),
        check_vma=False,
    )
```

```python
import math

import jax
import jax.numpy as jnp
from jax import lax
from jax.sharding import PartitionSpec as P


HD = 128
DOM = ("dh", "dc")


def attend(queries, scaled, seg_keys, seg_values, pre_keys, pre_values):
    factor = 1.0 / math.sqrt(queries.shape[-1])
    score_pre = (
        jnp.einsum("bikgd,bjkd->bkgij", queries, pre_keys, preferred_element_type=jnp.float32)
        * factor
    )
    score_seg = (
        jnp.einsum("bikgd,bjkd->bkgij", queries, seg_keys, preferred_element_type=jnp.float32)
        * factor
    )
    length = queries.shape[1]
    causal = lax.broadcasted_iota(jnp.int32, (length, length), 0) >= lax.broadcasted_iota(
        jnp.int32, (length, length), 1
    )
    score_seg = jnp.where(causal, score_seg, -jnp.inf)
    row_max = jnp.maximum(jnp.max(score_pre, -1), jnp.max(score_seg, -1))[..., None]
    exp_pre = jnp.exp(score_pre - row_max)
    exp_seg = jnp.exp(score_seg - row_max)
    denominator = (jnp.sum(exp_pre, -1) + jnp.sum(exp_seg, -1))[..., None]
    prob_pre = exp_pre / denominator
    prob_seg = exp_seg / denominator
    dprob_pre = jnp.einsum(
        "bikgd,bjkd->bkgij", scaled, pre_values, preferred_element_type=jnp.float32
    )
    dprob_seg = jnp.einsum(
        "bikgd,bjkd->bkgij", scaled, seg_values, preferred_element_type=jnp.float32
    )
    row_delta = (jnp.sum(prob_pre * dprob_pre, -1) + jnp.sum(prob_seg * dprob_seg, -1))[..., None]
    dscore_pre = (prob_pre * (dprob_pre - row_delta)).astype(jnp.bfloat16)
    dscore_seg = (prob_seg * (dprob_seg - row_delta)).astype(jnp.bfloat16)
    grad_q = (
        jnp.einsum("bkgij,bjkd->bikgd", dscore_pre, pre_keys, preferred_element_type=jnp.float32)
        + jnp.einsum("bkgij,bjkd->bikgd", dscore_seg, seg_keys, preferred_element_type=jnp.float32)
    ) * factor
    grad_pk = (
        jnp.einsum("bkgij,bikgd->bjkd", dscore_pre, queries, preferred_element_type=jnp.float32)
        * factor
    )
    grad_pv = jnp.einsum(
        "bkgij,bikgd->bjkd",
        prob_pre.astype(jnp.bfloat16),
        scaled,
        preferred_element_type=jnp.float32,
    )
    grad_sk = (
        jnp.einsum("bkgij,bikgd->bjkd", dscore_seg, queries, preferred_element_type=jnp.float32)
        * factor
    )
    grad_sv = jnp.einsum(
        "bkgij,bikgd->bjkd",
        prob_seg.astype(jnp.bfloat16),
        scaled,
        preferred_element_type=jnp.float32,
    )
    return (
        grad_q.astype(jnp.bfloat16),
        grad_sk.astype(jnp.bfloat16),
        grad_sv.astype(jnp.bfloat16),
        grad_pk,
        grad_pv,
    )


TP_RING = (0, 2, 4, 6, 7, 5, 3, 1)


def gather_ring(block):
    size = len(TP_RING)
    ahead = size // 2
    behind = size - 1 - ahead
    forward = [(TP_RING[i], TP_RING[(i + 1) % size]) for i in range(size)]
    backward = [(TP_RING[(i + 1) % size], TP_RING[i]) for i in range(size)]
    pieces = [block]
    moving = block
    for _ in range(ahead):
        moving = lax.ppermute(moving, "tp", forward)
        pieces.append(moving)
    moving = block
    for _ in range(behind):
        moving = lax.ppermute(moving, "tp", backward)
        pieces.append(moving)
    offsets = [0] + [-(s + 1) for s in range(ahead)] + [s + 1 for s in range(behind)]
    ring = jnp.array(TP_RING, jnp.int32)
    place = jnp.zeros((size,), jnp.int32).at[ring].set(jnp.arange(size, dtype=jnp.int32))
    here = place[lax.axis_index("tp")]
    order = ring[(here + jnp.array(offsets, jnp.int32)) % size]
    stacked = jnp.zeros((size,) + block.shape, block.dtype)
    for slot, piece in enumerate(pieces):
        stacked = lax.dynamic_update_index_in_dim(stacked, piece, order[slot], 0)
    return stacked


def pair_sum(block):
    mine = lax.axis_index("dc")
    kept = lax.dynamic_index_in_dim(block, mine, axis=0, keepdims=False)
    sent = lax.dynamic_index_in_dim(block, 1 - mine, axis=0, keepdims=False)
    other = lax.ppermute(sent, "dc", [(0, 1), (1, 0)])
    return kept.astype(jnp.float32) + other.astype(jnp.float32)


def local(
    hidden_in,
    query_weight,
    segment_keys,
    segment_values,
    prefix_keys,
    prefix_values,
    ancestors,
    twist_weights,
    out_grad,
):
    particles_here = hidden_in.shape[0]
    length = hidden_in.shape[1]
    owners = lax.axis_size(DOM)
    features = gather_ring(hidden_in)
    blocks = features.shape[0]
    width_in = hidden_in.shape[2]
    token_blocks = features.reshape(blocks, particles_here * length, width_in)
    width_q = query_weight.shape[1]
    width_kv = segment_keys.shape[2]
    kv_heads = width_kv // HD
    group_size = width_q // width_kv
    prefix = prefix_keys.shape[1]
    every_weight = lax.all_gather(query_weight, DOM, axis=0, tiled=True)
    weight_blocks = every_weight.reshape(blocks, width_in, width_q)
    queries = jnp.einsum(
        "ktd,kdq->tq",
        token_blocks,
        weight_blocks,
        preferred_element_type=jnp.float32,
    ).astype(jnp.bfloat16)
    queries = queries.reshape(particles_here, length, width_q)
    scaled = (out_grad.astype(jnp.float32) * twist_weights[:, None, None]).astype(jnp.bfloat16)

    chips = lax.axis_size("dh")
    cores = lax.axis_size("dc")
    own_kv = jnp.concatenate([prefix_keys, prefix_values], axis=2)
    half_kv = lax.all_to_all(
        jnp.broadcast_to(own_kv, (chips,) + own_kv.shape[1:]),
        "dh",
        split_axis=0,
        concat_axis=0,
        tiled=True,
    )
    other_kv = lax.ppermute(half_kv, "dc", [(0, 1), (1, 0)])
    on_this_core = (ancestors % cores == lax.axis_index("dc"))[:, None, None]
    picked = jnp.where(
        on_this_core,
        jnp.take(half_kv, ancestors // cores, axis=0),
        jnp.take(other_kv, ancestors // cores, axis=0),
    )
    pre_keys = picked[:, :, :width_kv]
    pre_values = picked[:, :, width_kv:]

    grad_q, grad_sk, grad_sv, grad_pk, grad_pv = attend(
        queries.reshape(particles_here, length, kv_heads, group_size, HD),
        scaled.reshape(particles_here, length, kv_heads, group_size, HD),
        segment_keys.reshape(particles_here, length, kv_heads, HD),
        segment_values.reshape(particles_here, length, kv_heads, HD),
        pre_keys.reshape(particles_here, prefix, kv_heads, HD),
        pre_values.reshape(particles_here, prefix, kv_heads, HD),
    )
    grad_rows = grad_q.reshape(particles_here * length, width_q)
    partial = jnp.einsum(
        "ktd,tq->kdq", token_blocks, grad_rows, preferred_element_type=jnp.float32
    ).astype(jnp.bfloat16)
    grad_weight = lax.psum_scatter(
        partial.reshape(blocks * width_in, width_q),
        DOM,
        scatter_dimension=0,
        tiled=True,
    )
    grad_pkv = jnp.concatenate(
        [
            grad_pk.reshape(particles_here, prefix, width_kv),
            grad_pv.reshape(particles_here, prefix, width_kv),
        ],
        axis=2,
    )
    core_major = jnp.arange(owners, dtype=jnp.int32).reshape(chips, cores).T.reshape(owners)
    onehot = (core_major[:, None] == ancestors[None, :]).astype(jnp.float32)
    outgoing = jnp.einsum(
        "ap,pjc->ajc", onehot, grad_pkv, precision=lax.Precision.HIGHEST
    )
    on_chip = pair_sum(outgoing.astype(jnp.bfloat16).reshape((cores, chips) + outgoing.shape[1:]))
    incoming = lax.all_to_all(
        on_chip.astype(jnp.bfloat16),
        "dh",
        split_axis=0,
        concat_axis=0,
        tiled=True,
    )
    summed = jnp.sum(incoming.astype(jnp.float32), axis=0)
    grad_pre_keys = summed[None, :, :width_kv]
    grad_pre_values = summed[None, :, width_kv:]
    grad_seg_keys = grad_sk.reshape(particles_here, length, width_kv)
    grad_seg_values = grad_sv.reshape(particles_here, length, width_kv)
    return (grad_weight, grad_seg_keys, grad_seg_values, grad_pre_keys, grad_pre_values)


def solution(mesh):
    split = jax.sharding.Mesh(
        mesh.devices.reshape(mesh.shape["dom"] // 2, 2, mesh.shape["tp"]), ("dh", "dc", "tp")
    )
    return jax.shard_map(
        local,
        mesh=split,
        in_specs=(
            P(DOM, None, "tp"),
            P(DOM, "tp"),
            P(DOM, None, "tp"),
            P(DOM, None, "tp"),
            P(DOM, None, "tp"),
            P(DOM, None, "tp"),
            P(DOM),
            P(DOM),
            P(DOM, None, "tp"),
        ),
        out_specs=(
            P(DOM, "tp"),
            P(DOM, None, "tp"),
            P(DOM, None, "tp"),
            P(DOM, None, "tp"),
            P(DOM, None, "tp"),
        ),
        check_vma=False,
    )
```
